512 devices in a mesh: dp: 32 (over y, z_hi, core), mp: 16 (over z_lo, x).
Axes of the slice: x: 4, y: 4, z: 16 (z_hi: 4, z_lo: 4; z = z_hi * 4 + z_lo), core: 2. Of those that a mesh axis runs over, the one named last changes fastest.
Arguments:
- inputs: bfloat16 [16384, 4096], P('mp', 'dp'), may hold values from -6 to 6
- cotangent: bfloat16 [16384, 4096], P('mp', 'dp'), may hold values from -6 to 6
- r_factor: bfloat16 [1, 128, 128, 128], P(None, 'mp'), may hold values from -0.5 to 0.5
- l_factor: bfloat16 [1, 128, 128, 128], P(None, 'mp'), may hold values from -0.5 to 0.5
Outputs:
- outputs: bfloat16 [16384, 4096], P('mp', 'dp')
- grad_inputs: bfloat16 [16384, 4096], P('mp', 'dp')
- grad_r: float32 [1, 128, 128, 128], P(None, 'mp', 'dp')
- grad_l: float32 [1, 128, 128, 128], P(None, 'mp', 'dp')
The draws below stay inside these ranges and needn't reach their ends.
All inputs are finite; a program needn't handle non-finite values.
Results may differ from the reference program's by a relative error of at most 0.0063.
Values may be sent and summed in bfloat16 or wider, within the bound.
No kernel may reach another device: no remote copies, remote signals or barrier semaphores. Data moves between devices by JAX's collectives and lax.ppermute only.
A program may use at most 64 MiB of HBM per device.

```python
import jax
import jax.numpy as jnp
from jax import lax

BLK = 128
WIDTH = 16384
LAYERS = 1
TOK_DEV = 128
TOKENS = 4096


def block_levels(rng, shape, cuts, smallest, largest):
    gain, own = 1.0, jax.random.fold_in(rng, 6)
    for position, blocks in cuts:
        draws = jnp.exp(jax.random.uniform(jax.random.fold_in(own, position), (blocks,), jnp.float32, smallest / len(cuts), largest / len(cuts)))
        gain = gain * jnp.repeat(draws, shape[position] // blocks).reshape([-1 if axis == position else 1 for axis in range(len(shape))])
    return gain


def centred(own_key, extent, deviation, reach, split=(), dtype=jnp.bfloat16):
    drawn = jax.random.normal(own_key, extent, jnp.float32) * deviation
    if len(split) > 0:
        drawn = block_levels(own_key, extent, split, -0.22, 0.18) * drawn
    return jnp.clip(drawn, min=-reach, max=reach).astype(dtype)


def setup_inputs(seed: int = 0) -> dict:
    splits = jax.random.split(jax.random.key(seed), 5)
    inputs = centred(splits[0], (WIDTH, TOKENS), 1.0, 6.0, ((0, 16), (1, 32)))
    cotangent = centred(splits[1], (WIDTH, TOKENS), 1.0, 6.0, ((0, 16), (1, 32)))
    r_factor = centred(splits[2], (LAYERS, BLK, BLK, BLK), BLK ** -0.5, 0.5, ((1, 16),))
    l_factor = centred(splits[3], (LAYERS, BLK, BLK, BLK), BLK ** -0.5, 0.5, ((1, 16),))
    return dict(inputs=inputs, cotangent=cotangent, r_factor=r_factor, l_factor=l_factor)


def activate(values):
    return jax.nn.gelu(values, approximate=True)

def reference(inputs, cotangent, r_factor, l_factor):
    count = TOKENS // TOK_DEV
    f32 = jnp.float32
    bf16 = jnp.bfloat16
    inputs_b = inputs.reshape(BLK, BLK, count, TOK_DEV).transpose(2, 0, 1, 3)
    cotan_b = cotangent.reshape(BLK, BLK, count, TOK_DEV).transpose(2, 0, 1, 3)
    rights = r_factor.astype(f32)
    lefts = l_factor.astype(f32)

    def block_step(totals, piece_pair):
        sum_r, sum_l = totals
        current, grad_now = piece_pair
        saved = []
        for layer_index in range(LAYERS):
            first_out = jnp.einsum('ikt,ikj->ijt', current.astype(f32), rights[layer_index]).astype(bf16)
            pre_act = jnp.einsum('ijt,jim->jmt', first_out.astype(f32), lefts[layer_index])
            saved.append((current, first_out, pre_act))
            current = activate(pre_act).astype(bf16)
        result = current
        for layer_index in reversed(range(LAYERS)):
            layer_in, first_out, pre_act = saved[layer_index]
            back_fn = jax.vjp(activate, pre_act)[1]
            grad_pre = back_fn(grad_now.astype(f32))[0].astype(bf16)
            sum_l = sum_l.at[layer_index].add(jnp.einsum('ijt,jmt->jim', first_out.astype(f32), grad_pre.astype(f32)))
            grad_first = jnp.einsum('jmt,jim->ijt', grad_pre.astype(f32), lefts[layer_index]).astype(bf16)
            sum_r = sum_r.at[layer_index].add(jnp.einsum('ikt,ijt->ikj', layer_in.astype(f32), grad_first.astype(f32)))
            grad_now = jnp.einsum('ijt,ikj->ikt', grad_first.astype(f32), rights[layer_index]).astype(bf16)
        return ((sum_r, sum_l), (result, grad_now))
    zeros = jnp.zeros((LAYERS, BLK, BLK, BLK), f32)
    (sum_r, sum_l), (results, grads) = lax.scan(block_step, (zeros, zeros), (inputs_b, cotan_b))
    scale = float(TOKENS) ** (-0.5)
    outputs = results.transpose(1, 2, 0, 3).reshape(WIDTH, TOKENS)
    grad_inputs = grads.transpose(1, 2, 0, 3).reshape(WIDTH, TOKENS)
    return (outputs, grad_inputs, sum_r * scale, sum_l * scale)
```

```python
import jax
import jax.numpy as jnp
from jax import lax
from jax.sharding import PartitionSpec as P

LAYERS = 1


def activate(values):
    return jax.nn.gelu(values, approximate=True)


def second_product(received, left):
    return jnp.einsum("ijt,jim->jmt", received, left, preferred_element_type=jnp.float32)


def left_apply(left, received):
    return (received, second_product(received, left))


def first_product(current, right):
    return jnp.einsum("ikt,ikj->ijt", current, right, preferred_element_type=jnp.float32).astype(
        jnp.bfloat16
    )


def forward_layer(current, right, left):
    first_out = first_product(current, right)
    return left_apply(
        left, lax.all_to_all(first_out, "mp", split_axis=1, concat_axis=0, tiled=True)
    )


def dp_stages(mesh):
    names = list(mesh.axis_names)
    devs = mesh.devices
    devs = devs.transpose([names.index("dp")] + [k for k in range(devs.ndim) if names[k] != "dp"])
    column = [devs[(d,) + (0,) * (devs.ndim - 1)] for d in range(devs.shape[0])]
    count = len(column)

    def key(dev):
        coords = tuple(getattr(dev, "coords", (dev.id,)))
        return coords + (getattr(dev, "core_on_chip", 0),)

    keys = [key(dev) for dev in column]
    stages = []
    stride = 1
    while stride < count:
        base = keys[0]
        step = keys[stride]
        varying = [a for a in range(len(base)) if base[a] != step[a]]
        size = 1
        while size * stride < count:
            probe = keys[size * stride]
            if [a for a in range(len(base)) if base[a] != probe[a]] != varying:
                break
            size += 1
        if count % (size * stride) != 0 or size < 2:
            size = count // stride
        distance = 0 if varying == [len(base) - 1] else max(
            abs(step[a] - base[a]) for a in varying
        )
        stages.append((distance, size, stride))
        stride *= size
    return stages


def staged_reduce_scatter(term, stages, count):
    lead = term.shape[:-2]
    rows, cols = term.shape[-2:]
    piece = rows // count
    by_stride = sorted(stages, key=lambda s: -s[2])
    digit_sizes = [s[1] for s in by_stride]
    x = term.reshape(lead + tuple(digit_sizes) + (piece, cols))
    order = sorted(stages, key=lambda s: (s[0], s[2]))
    nlead = len(lead)
    perm = [nlead + by_stride.index(s) for s in order]
    x = x.transpose(perm + list(range(nlead)) + list(range(nlead + len(stages), x.ndim)))
    me = lax.axis_index("dp")
    for _, size, stride in order:
        mine = (me // stride) % size
        total = lax.dynamic_index_in_dim(x, mine, 0, keepdims=False)
        for shift in range(1, size):
            pairs = []
            for d in range(count):
                own = (d // stride) % size
                pairs.append((d, d + (((own + shift) % size) - own) * stride))
            send = lax.dynamic_index_in_dim(x, (mine + shift) % size, 0, keepdims=False)
            total = total + lax.ppermute(send, "dp", perm=pairs)
        x = total
    return x


def shards(stages, inputs, cotangent, r_factor, l_factor):
    block_count = r_factor.shape[1]
    block_size = r_factor.shape[2]
    tokens_here = inputs.shape[1]
    dp_count = lax.axis_size("dp")
    scale = float(dp_count * tokens_here) ** (-0.5)
    current = inputs.reshape(block_count, block_size, tokens_here)
    layer_index = 0
    received, pre_act = forward_layer(current, r_factor[layer_index], l_factor[layer_index])
    saved = [(current, received, pre_act)]
    current = activate(pre_act).astype(jnp.bfloat16)
    outputs = current.reshape(block_count * block_size, tokens_here)
    grad_now = cotangent.reshape(block_count, block_size, tokens_here)
    parts_r = [None] * LAYERS
    parts_l = [None] * LAYERS
    for layer_index in reversed(range(LAYERS)):
        right = r_factor[layer_index]
        left = l_factor[layer_index]
        layer_in = saved[layer_index][0]
        received = saved[layer_index][1]
        pre_act = saved[layer_index][2]
        back_fn = jax.vjp(activate, pre_act)[1]
        grad_pre = back_fn(grad_now.astype(jnp.float32))[0].astype(jnp.bfloat16)
        term_l = (
            jnp.einsum("ijt,jmt->jim", received, grad_pre, preferred_element_type=jnp.float32)
            * scale
        )
        grad_first = jnp.einsum(
            "jmt,jim->ijt", grad_pre, left, preferred_element_type=jnp.float32
        ).astype(jnp.bfloat16)

        def apply_back(returned, right=right):
            spread = jnp.einsum("ijt,ikj->ikt", returned, right, preferred_element_type=jnp.float32)
            return (returned, spread.astype(jnp.bfloat16))

        returned, grad_now = apply_back(
            lax.all_to_all(grad_first, "mp", split_axis=0, concat_axis=1, tiled=True)
        )
        term_r = (
            jnp.einsum("ikt,ijt->ikj", layer_in, returned, preferred_element_type=jnp.float32)
            * scale
        )
        both = staged_reduce_scatter(jnp.stack([term_l, term_r], 0), stages, dp_count)
        parts_l[layer_index] = both[0]
        parts_r[layer_index] = both[1]
    stack_r = jnp.stack(parts_r, 0)
    stack_l = jnp.stack(parts_l, 0)
    grad_inputs = grad_now.reshape(block_count * block_size, tokens_here)
    return (outputs, grad_inputs, stack_r, stack_l)


def solution(mesh):
    stages = dp_stages(mesh)
    placed = (P("mp", "dp"), P("mp", "dp"), P(None, "mp", None, None), P(None, "mp", None, None))

    def body(*args):
        return shards(stages, *args)

    return jax.shard_map(
        body,
        mesh=mesh,
        in_specs=placed,
        out_specs=(
            P("mp", "dp"),
            P("mp", "dp"),
            P(None, "mp", "dp", None),
            P(None, "mp", "dp", None),
        ),
        check_vma=False,
    )
```

```python
import jax
import jax.numpy as jnp
from jax import lax
from jax.sharding import PartitionSpec as P

LAYERS = 1


def activate(values):
    return jax.nn.gelu(values, approximate=True)


def second_product(received, left):
    return jnp.einsum("ijt,jim->jmt", received, left, preferred_element_type=jnp.float32)


def left_apply(left, received):
    return (received, second_product(received, left))


def first_product(current, right):
    return jnp.einsum("ikt,ikj->ijt", current, right, preferred_element_type=jnp.float32).astype(
        jnp.bfloat16
    )


def forward_layer(current, right, left):
    first_out = first_product(current, right)
    return left_apply(
        left, lax.all_to_all(first_out, "mp", split_axis=1, concat_axis=0, tiled=True)
    )


def dp_stages(mesh):
    names = list(mesh.axis_names)
    devs = mesh.devices
    devs = devs.transpose([names.index("dp")] + [k for k in range(devs.ndim) if names[k] != "dp"])
    column = [devs[(d,) + (0,) * (devs.ndim - 1)] for d in range(devs.shape[0])]
    count = len(column)

    def key(dev):
        coords = tuple(getattr(dev, "coords", (dev.id,)))
        return coords + (getattr(dev, "core_on_chip", 0),)

    keys = [key(dev) for dev in column]
    stages = []
    stride = 1
    while stride < count:
        base = keys[0]
        step = keys[stride]
        varying = [a for a in range(len(base)) if base[a] != step[a]]
        size = 1
        while size * stride < count:
            probe = keys[size * stride]
            if [a for a in range(len(base)) if base[a] != probe[a]] != varying:
                break
            size += 1
        if count % (size * stride) != 0 or size < 2:
            size = count // stride
        distance = 0 if varying == [len(base) - 1] else max(
            abs(step[a] - base[a]) for a in varying
        )
        stages.append((distance, size, stride))
        stride *= size
    return stages


def staged_reduce_scatter(term, stages, count):
    lead = term.shape[:-2]
    rows, cols = term.shape[-2:]
    piece = rows // count
    by_stride = sorted(stages, key=lambda s: -s[2])
    digit_sizes = [s[1] for s in by_stride]
    x = term.reshape(lead + tuple(digit_sizes) + (piece, cols))
    order = sorted(stages, key=lambda s: (s[0], s[2]))
    nlead = len(lead)
    perm = [nlead + by_stride.index(s) for s in order]
    x = x.transpose(perm + list(range(nlead)) + list(range(nlead + len(stages), x.ndim)))
    me = lax.axis_index("dp")
    for distance, size, stride in order:
        mine = (me // stride) % size

        def pick(shift, x=x, mine=mine, size=size):
            return lax.dynamic_index_in_dim(x, (mine + shift) % size, 0, keepdims=False)

        def pairs(shift, size=size, stride=stride):
            out = []
            for d in range(count):
                own = (d // stride) % size
                out.append((d, d + (((own + shift) % size) - own) * stride))
            return out

        if size == 4 and distance > 1:
            ahead = lax.ppermute(jnp.stack([pick(1), pick(2)], 0), "dp", perm=pairs(1))
            behind = lax.ppermute(pick(-1), "dp", perm=pairs(-1))
            relayed = lax.ppermute(ahead[1], "dp", perm=pairs(1))
            x = pick(0) + ahead[0] + behind + relayed
            continue
        total = pick(0)
        for shift in range(1, size):
            total = total + lax.ppermute(pick(shift), "dp", perm=pairs(shift))
        x = total
    return x


def shards(stages, inputs, cotangent, r_factor, l_factor):
    block_count = r_factor.shape[1]
    block_size = r_factor.shape[2]
    tokens_here = inputs.shape[1]
    dp_count = lax.axis_size("dp")
    scale = float(dp_count * tokens_here) ** (-0.5)
    current = inputs.reshape(block_count, block_size, tokens_here)
    layer_index = 0
    received, pre_act = forward_layer(current, r_factor[layer_index], l_factor[layer_index])
    saved = [(current, received, pre_act)]
    current = activate(pre_act).astype(jnp.bfloat16)
    outputs = current.reshape(block_count * block_size, tokens_here)
    grad_now = cotangent.reshape(block_count, block_size, tokens_here)
    parts_r = [None] * LAYERS
    parts_l = [None] * LAYERS
    for layer_index in reversed(range(LAYERS)):
        right = r_factor[layer_index]
        left = l_factor[layer_index]
        layer_in = saved[layer_index][0]
        received = saved[layer_index][1]
        pre_act = saved[layer_index][2]
        back_fn = jax.vjp(activate, pre_act)[1]
        grad_pre = back_fn(grad_now.astype(jnp.float32))[0].astype(jnp.bfloat16)
        term_l = (
            jnp.einsum("ijt,jmt->jim", received, grad_pre, preferred_element_type=jnp.float32)
            * scale
        )
        grad_first = jnp.einsum(
            "jmt,jim->ijt", grad_pre, left, preferred_element_type=jnp.float32
        ).astype(jnp.bfloat16)

        def apply_back(returned, right=right):
            spread = jnp.einsum("ijt,ikj->ikt", returned, right, preferred_element_type=jnp.float32)
            return (returned, spread.astype(jnp.bfloat16))

        returned, grad_now = apply_back(
            lax.all_to_all(grad_first, "mp", split_axis=0, concat_axis=1, tiled=True)
        )
        term_r = (
            jnp.einsum("ikt,ijt->ikj", layer_in, returned, preferred_element_type=jnp.float32)
            * scale
        )
        both = staged_reduce_scatter(jnp.stack([term_l, term_r], 0), stages, dp_count)
        parts_l[layer_index] = both[0]
        parts_r[layer_index] = both[1]
    stack_r = jnp.stack(parts_r, 0)
    stack_l = jnp.stack(parts_l, 0)
    grad_inputs = grad_now.reshape(block_count * block_size, tokens_here)
    return (outputs, grad_inputs, stack_r, stack_l)


def solution(mesh):
    stages = dp_stages(mesh)
    placed = (P("mp", "dp"), P("mp", "dp"), P(None, "mp", None, None), P(None, "mp", None, None))

    def body(*args):
        return shards(stages, *args)

    return jax.shard_map(
        body,
        mesh=mesh,
        in_specs=placed,
        out_specs=(
            P("mp", "dp"),
            P("mp", "dp"),
            P(None, "mp", "dp", None),
            P(None, "mp", "dp", None),
        ),
        check_vma=False,
    )
```

```python
import jax
import jax.numpy as jnp
from jax import lax
from jax.sharding import PartitionSpec as P

LAYERS = 1


def activate(values):
    return jax.nn.gelu(values, approximate=True)


def second_product(received, left):
    return jnp.einsum("ijt,jim->jmt", received, left, preferred_element_type=jnp.float32)


def left_apply(left, received):
    return (received, second_product(received, left))


def first_product(current, right):
    return jnp.einsum("ikt,ikj->ijt", current, right, preferred_element_type=jnp.float32).astype(
        jnp.bfloat16
    )


def forward_layer(current, right, left):
    first_out = first_product(current, right)
    return left_apply(
        left, lax.all_to_all(first_out, "mp", split_axis=1, concat_axis=0, tiled=True)
    )


def dp_stages(mesh):
    names = list(mesh.axis_names)
    devs = mesh.devices
    devs = devs.transpose([names.index("dp")] + [k for k in range(devs.ndim) if names[k] != "dp"])
    column = [devs[(d,) + (0,) * (devs.ndim - 1)] for d in range(devs.shape[0])]
    count = len(column)

    def key(dev):
        coords = tuple(getattr(dev, "coords", (dev.id,)))
        return coords + (getattr(dev, "core_on_chip", 0),)

    keys = [key(dev) for dev in column]
    stages = []
    stride = 1
    while stride < count:
        base = keys[0]
        step = keys[stride]
        varying = [a for a in range(len(base)) if base[a] != step[a]]
        size = 1
        while size * stride < count:
            probe = keys[size * stride]
            if [a for a in range(len(base)) if base[a] != probe[a]] != varying:
                break
            size += 1
        if count % (size * stride) != 0 or size < 2:
            size = count // stride
        distance = 0 if varying == [len(base) - 1] else max(
            abs(step[a] - base[a]) for a in varying
        )
        stages.append((distance, size, stride))
        stride *= size
    return stages


def staged_reduce_scatter(term, stages, count):
    lead = term.shape[:-2]
    rows, cols = term.shape[-2:]
    piece = rows // count
    by_stride = sorted(stages, key=lambda s: -s[2])
    digit_sizes = [s[1] for s in by_stride]
    x = term.reshape(lead + tuple(digit_sizes) + (piece, cols))
    order = sorted(stages, key=lambda s: (s[0], s[2]))
    nlead = len(lead)
    perm = [nlead + by_stride.index(s) for s in order]
    x = x.transpose(perm + list(range(nlead)) + list(range(nlead + len(stages), x.ndim)))
    me = lax.axis_index("dp")
    for distance, size, stride in order:
        mine = (me // stride) % size

        def pick(shift, x=x, mine=mine, size=size):
            return lax.dynamic_index_in_dim(x, (mine + shift) % size, 0, keepdims=False)

        def pairs(shift, size=size, stride=stride):
            out = []
            for d in range(count):
                own = (d // stride) % size
                out.append((d, d + (((own + shift) % size) - own) * stride))
            return out

        if size == 4 and distance > 1:
            ahead = lax.ppermute(jnp.stack([pick(1), pick(2)], 0), "dp", perm=pairs(1))
            behind = lax.ppermute(pick(-1), "dp", perm=pairs(-1))
            relayed = lax.ppermute(ahead[1], "dp", perm=pairs(1))
            x = pick(0) + ahead[0] + behind + relayed
            continue
        total = pick(0)
        for shift in range(1, size):
            sent = lax.ppermute(pick(shift).astype(jnp.bfloat16), "dp", perm=pairs(shift))
            total = total + sent.astype(total.dtype)
        x = total
    return x


def shards(stages, inputs, cotangent, r_factor, l_factor):
    block_count = r_factor.shape[1]
    block_size = r_factor.shape[2]
    tokens_here = inputs.shape[1]
    dp_count = lax.axis_size("dp")
    scale = float(dp_count * tokens_here) ** (-0.5)
    current = inputs.reshape(block_count, block_size, tokens_here)
    layer_index = 0
    received, pre_act = forward_layer(current, r_factor[layer_index], l_factor[layer_index])
    saved = [(current, received, pre_act)]
    current = activate(pre_act).astype(jnp.bfloat16)
    outputs = current.reshape(block_count * block_size, tokens_here)
    grad_now = cotangent.reshape(block_count, block_size, tokens_here)
    parts_r = [None] * LAYERS
    parts_l = [None] * LAYERS
    for layer_index in reversed(range(LAYERS)):
        right = r_factor[layer_index]
        left = l_factor[layer_index]
        layer_in = saved[layer_index][0]
        received = saved[layer_index][1]
        pre_act = saved[layer_index][2]
        back_fn = jax.vjp(activate, pre_act)[1]
        grad_pre = back_fn(grad_now.astype(jnp.float32))[0].astype(jnp.bfloat16)
        term_l = (
            jnp.einsum("ijt,jmt->jim", received, grad_pre, preferred_element_type=jnp.float32)
            * scale
        )
        grad_first = jnp.einsum(
            "jmt,jim->ijt", grad_pre, left, preferred_element_type=jnp.float32
        ).astype(jnp.bfloat16)

        def apply_back(returned, right=right):
            spread = jnp.einsum("ijt,ikj->ikt", returned, right, preferred_element_type=jnp.float32)
            return (returned, spread.astype(jnp.bfloat16))

        returned, grad_now = apply_back(
            lax.all_to_all(grad_first, "mp", split_axis=0, concat_axis=1, tiled=True)
        )
        term_r = (
            jnp.einsum("ikt,ijt->ikj", layer_in, returned, preferred_element_type=jnp.float32)
            * scale
        )
        both = staged_reduce_scatter(jnp.stack([term_l, term_r], 0), stages, dp_count)
        parts_l[layer_index] = both[0]
        parts_r[layer_index] = both[1]
    stack_r = jnp.stack(parts_r, 0)
    stack_l = jnp.stack(parts_l, 0)
    grad_inputs = grad_now.reshape(block_count * block_size, tokens_here)
    return (outputs, grad_inputs, stack_r, stack_l)


def solution(mesh):
    stages = dp_stages(mesh)
    placed = (P("mp", "dp"), P("mp", "dp"), P(None, "mp", None, None), P(None, "mp", None, None))

    def body(*args):
        return shards(stages, *args)

    return jax.shard_map(
        body,
        mesh=mesh,
        in_specs=placed,
        out_specs=(
            P("mp", "dp"),
            P("mp", "dp"),
            P(None, "mp", "dp", None),
            P(None, "mp", "dp", None),
        ),
        check_vma=False,
    )
```

```python
import jax
import jax.numpy as jnp
from jax import lax
from jax.sharding import PartitionSpec as P

LAYERS = 1


def activate(values):
    return jax.nn.gelu(values, approximate=True)


def second_product(received, left):
    return jnp.einsum("ijt,jim->jmt", received, left, preferred_element_type=jnp.float32)


def left_apply(left, received):
    return (received, second_product(received, left))


def first_product(current, right):
    return jnp.einsum("ikt,ikj->ijt", current, right, preferred_element_type=jnp.float32).astype(
        jnp.bfloat16
    )


def forward_layer(current, right, left):
    first_out = first_product(current, right)
    return left_apply(
        left, lax.all_to_all(first_out, "mp", split_axis=1, concat_axis=0, tiled=True)
    )


def dp_stages(mesh):
    names = list(mesh.axis_names)
    devs = mesh.devices
    devs = devs.transpose([names.index("dp")] + [k for k in range(devs.ndim) if names[k] != "dp"])
    column = [devs[(d,) + (0,) * (devs.ndim - 1)] for d in range(devs.shape[0])]
    count = len(column)

    def key(dev):
        coords = tuple(getattr(dev, "coords", (dev.id,)))
        return coords + (getattr(dev, "core_on_chip", 0),)

    keys = [key(dev) for dev in column]
    stages = []
    stride = 1
    while stride < count:
        base = keys[0]
        step = keys[stride]
        varying = [a for a in range(len(base)) if base[a] != step[a]]
        size = 1
        while size * stride < count:
            probe = keys[size * stride]
            if [a for a in range(len(base)) if base[a] != probe[a]] != varying:
                break
            size += 1
        if count % (size * stride) != 0 or size < 2:
            size = count // stride
        distance = 0 if varying == [len(base) - 1] else max(
            abs(step[a] - base[a]) for a in varying
        )
        stages.append((distance, size, stride))
        stride *= size
    return stages


def staged_reduce_scatter(term, stages, count):
    lead = term.shape[:-2]
    rows, cols = term.shape[-2:]
    piece = rows // count
    by_stride = sorted(stages, key=lambda s: -s[2])
    digit_sizes = [s[1] for s in by_stride]
    x = term.reshape(lead + tuple(digit_sizes) + (piece, cols))
    order = sorted(stages, key=lambda s: (s[0], s[2]))
    nlead = len(lead)
    perm = [nlead + by_stride.index(s) for s in order]
    x = x.transpose(perm + list(range(nlead)) + list(range(nlead + len(stages), x.ndim)))
    me = lax.axis_index("dp")
    for distance, size, stride in order:
        mine = (me // stride) % size

        def pick(shift, x=x, mine=mine, size=size):
            return lax.dynamic_index_in_dim(x, (mine + shift) % size, 0, keepdims=False)

        def pairs(shift, size=size, stride=stride):
            out = []
            for d in range(count):
                own = (d // stride) % size
                out.append((d, d + (((own + shift) % size) - own) * stride))
            return out

        if size == 4 and distance > 1:
            ahead = lax.ppermute(jnp.stack([pick(1), pick(2)], 0), "dp", perm=pairs(1))
            behind = lax.ppermute(pick(-1), "dp", perm=pairs(-1))
            relayed = lax.ppermute(ahead[1], "dp", perm=pairs(1))
            x = pick(0) + ahead[0] + behind + relayed
            continue
        if size == 4:
            groups = []
            for d in range(count):
                if (d // stride) % size == 0:
                    groups.append([d + k * stride for k in range(size)])
            sent = lax.all_to_all(
                x.astype(jnp.bfloat16), "dp", 0, 0, tiled=True, axis_index_groups=groups
            )
            x = sent.astype(x.dtype).sum(0)
            continue
        total = pick(0)
        for shift in range(1, size):
            sent = lax.ppermute(pick(shift).astype(jnp.bfloat16), "dp", perm=pairs(shift))
            total = total + sent.astype(total.dtype)
        x = total
    return x


def shards(stages, inputs, cotangent, r_factor, l_factor):
    block_count = r_factor.shape[1]
    block_size = r_factor.shape[2]
    tokens_here = inputs.shape[1]
    dp_count = lax.axis_size("dp")
    scale = float(dp_count * tokens_here) ** (-0.5)
    current = inputs.reshape(block_count, block_size, tokens_here)
    layer_index = 0
    received, pre_act = forward_layer(current, r_factor[layer_index], l_factor[layer_index])
    saved = [(current, received, pre_act)]
    current = activate(pre_act).astype(jnp.bfloat16)
    outputs = current.reshape(block_count * block_size, tokens_here)
    grad_now = cotangent.reshape(block_count, block_size, tokens_here)
    parts_r = [None] * LAYERS
    parts_l = [None] * LAYERS
    for layer_index in reversed(range(LAYERS)):
        right = r_factor[layer_index]
        left = l_factor[layer_index]
        layer_in = saved[layer_index][0]
        received = saved[layer_index][1]
        pre_act = saved[layer_index][2]
        back_fn = jax.vjp(activate, pre_act)[1]
        grad_pre = back_fn(grad_now.astype(jnp.float32))[0].astype(jnp.bfloat16)
        term_l = (
            jnp.einsum("ijt,jmt->jim", received, grad_pre, preferred_element_type=jnp.float32)
            * scale
        )
        grad_first = jnp.einsum(
            "jmt,jim->ijt", grad_pre, left, preferred_element_type=jnp.float32
        ).astype(jnp.bfloat16)

        def apply_back(returned, right=right):
            spread = jnp.einsum("ijt,ikj->ikt", returned, right, preferred_element_type=jnp.float32)
            return (returned, spread.astype(jnp.bfloat16))

        returned, grad_now = apply_back(
            lax.all_to_all(grad_first, "mp", split_axis=0, concat_axis=1, tiled=True)
        )
        term_r = (
            jnp.einsum("ikt,ijt->ikj", layer_in, returned, preferred_element_type=jnp.float32)
            * scale
        )
        both = staged_reduce_scatter(jnp.stack([term_l, term_r], 0), stages, dp_count)
        parts_l[layer_index] = both[0]
        parts_r[layer_index] = both[1]
    stack_r = jnp.stack(parts_r, 0)
    stack_l = jnp.stack(parts_l, 0)
    grad_inputs = grad_now.reshape(block_count * block_size, tokens_here)
    return (outputs, grad_inputs, stack_r, stack_l)


def solution(mesh):
    stages = dp_stages(mesh)
    placed = (P("mp", "dp"), P("mp", "dp"), P(None, "mp", None, None), P(None, "mp", None, None))

    def body(*args):
        return shards(stages, *args)

    return jax.shard_map(
        body,
        mesh=mesh,
        in_specs=placed,
        out_specs=(
            P("mp", "dp"),
            P("mp", "dp"),
            P(None, "mp", "dp", None),
            P(None, "mp", "dp", None),
        ),
        check_vma=False,
    )
```

```python
import jax
import jax.numpy as jnp
from jax import lax
from jax.sharding import PartitionSpec as P

LAYERS = 1


def activate(values):
    return jax.nn.gelu(values, approximate=True)


def second_product(received, left):
    return jnp.einsum("ijt,jim->jmt", received, left, preferred_element_type=jnp.float32)


def left_apply(left, received):
    return (received, second_product(received, left))


def first_product(current, right):
    return jnp.einsum("ikt,ikj->ijt", current, right, preferred_element_type=jnp.float32).astype(
        jnp.bfloat16
    )


def forward_layer(current, right, left):
    first_out = first_product(current, right)
    return left_apply(
        left, lax.all_to_all(first_out, "mp", split_axis=1, concat_axis=0, tiled=True)
    )


def dp_stages(mesh):
    names = list(mesh.axis_names)
    devs = mesh.devices
    devs = devs.transpose([names.index("dp")] + [k for k in range(devs.ndim) if names[k] != "dp"])
    column = [devs[(d,) + (0,) * (devs.ndim - 1)] for d in range(devs.shape[0])]
    count = len(column)

    def key(dev):
        coords = tuple(getattr(dev, "coords", (dev.id,)))
        return coords + (getattr(dev, "core_on_chip", 0),)

    keys = [key(dev) for dev in column]
    stages = []
    stride = 1
    while stride < count:
        base = keys[0]
        step = keys[stride]
        varying = [a for a in range(len(base)) if base[a] != step[a]]
        size = 1
        while size * stride < count:
            probe = keys[size * stride]
            if [a for a in range(len(base)) if base[a] != probe[a]] != varying:
                break
            size += 1
        if count % (size * stride) != 0 or size < 2:
            size = count // stride
        distance = 0 if varying == [len(base) - 1] else max(
            abs(step[a] - base[a]) for a in varying
        )
        stages.append((distance, size, stride))
        stride *= size
    return stages


def staged_reduce_scatter(term, stages, count):
    lead = term.shape[:-2]
    rows, cols = term.shape[-2:]
    piece = rows // count
    by_stride = sorted(stages, key=lambda s: -s[2])
    digit_sizes = [s[1] for s in by_stride]
    x = term.reshape(lead + tuple(digit_sizes) + (piece, cols))
    order = sorted(stages, key=lambda s: (s[0], s[2]))
    nlead = len(lead)
    perm = [nlead + by_stride.index(s) for s in order]
    x = x.transpose(perm + list(range(nlead)) + list(range(nlead + len(stages), x.ndim)))
    me = lax.axis_index("dp")
    for distance, size, stride in order:
        mine = (me // stride) % size

        def pick(shift, x=x, mine=mine, size=size):
            return lax.dynamic_index_in_dim(x, (mine + shift) % size, 0, keepdims=False)

        def pairs(shift, size=size, stride=stride):
            out = []
            for d in range(count):
                own = (d // stride) % size
                out.append((d, d + (((own + shift) % size) - own) * stride))
            return out

        if size == 4 and distance > 1:
            wide = x.dtype
            ahead = jnp.stack([pick(1), pick(2)], 0).astype(jnp.bfloat16)
            ahead = lax.ppermute(ahead, "dp", perm=pairs(1))
            behind = lax.ppermute(pick(-1).astype(jnp.bfloat16), "dp", perm=pairs(-1))
            relayed = lax.ppermute(ahead[1], "dp", perm=pairs(1))
            x = pick(0) + ahead[0].astype(wide) + behind.astype(wide) + relayed.astype(wide)
            continue
        if size == 4:
            groups = []
            for d in range(count):
                if (d // stride) % size == 0:
                    groups.append([d + k * stride for k in range(size)])
            sent = lax.all_to_all(
                x.astype(jnp.bfloat16), "dp", 0, 0, tiled=True, axis_index_groups=groups
            )
            x = sent.astype(x.dtype).sum(0)
            continue
        total = pick(0)
        for shift in range(1, size):
            sent = lax.ppermute(pick(shift).astype(jnp.bfloat16), "dp", perm=pairs(shift))
            total = total + sent.astype(total.dtype)
        x = total
    return x


def shards(stages, inputs, cotangent, r_factor, l_factor):
    block_count = r_factor.shape[1]
    block_size = r_factor.shape[2]
    tokens_here = inputs.shape[1]
    dp_count = lax.axis_size("dp")
    scale = float(dp_count * tokens_here) ** (-0.5)
    current = inputs.reshape(block_count, block_size, tokens_here)
    layer_index = 0
    received, pre_act = forward_layer(current, r_factor[layer_index], l_factor[layer_index])
    saved = [(current, received, pre_act)]
    current = activate(pre_act).astype(jnp.bfloat16)
    outputs = current.reshape(block_count * block_size, tokens_here)
    grad_now = cotangent.reshape(block_count, block_size, tokens_here)
    parts_r = [None] * LAYERS
    parts_l = [None] * LAYERS
    for layer_index in reversed(range(LAYERS)):
        right = r_factor[layer_index]
        left = l_factor[layer_index]
        layer_in = saved[layer_index][0]
        received = saved[layer_index][1]
        pre_act = saved[layer_index][2]
        back_fn = jax.vjp(activate, pre_act)[1]
        grad_pre = back_fn(grad_now.astype(jnp.float32))[0].astype(jnp.bfloat16)
        term_l = (
            jnp.einsum("ijt,jmt->jim", received, grad_pre, preferred_element_type=jnp.float32)
            * scale
        )
        grad_first = jnp.einsum(
            "jmt,jim->ijt", grad_pre, left, preferred_element_type=jnp.float32
        ).astype(jnp.bfloat16)

        def apply_back(returned, right=right):
            spread = jnp.einsum("ijt,ikj->ikt", returned, right, preferred_element_type=jnp.float32)
            return (returned, spread.astype(jnp.bfloat16))

        returned, grad_now = apply_back(
            lax.all_to_all(grad_first, "mp", split_axis=0, concat_axis=1, tiled=True)
        )
        term_r = (
            jnp.einsum("ikt,ijt->ikj", layer_in, returned, preferred_element_type=jnp.float32)
            * scale
        )
        both = staged_reduce_scatter(jnp.stack([term_l, term_r], 0), stages, dp_count)
        parts_l[layer_index] = both[0]
        parts_r[layer_index] = both[1]
    stack_r = jnp.stack(parts_r, 0)
    stack_l = jnp.stack(parts_l, 0)
    grad_inputs = grad_now.reshape(block_count * block_size, tokens_here)
    return (outputs, grad_inputs, stack_r, stack_l)


def solution(mesh):
    stages = dp_stages(mesh)
    placed = (P("mp", "dp"), P("mp", "dp"), P(None, "mp", None, None), P(None, "mp", None, None))

    def body(*args):
        return shards(stages, *args)

    return jax.shard_map(
        body,
        mesh=mesh,
        in_specs=placed,
        out_specs=(
            P("mp", "dp"),
            P("mp", "dp"),
            P(None, "mp", "dp", None),
            P(None, "mp", "dp", None),
        ),
        check_vma=False,
    )
```

```python
import jax
import jax.numpy as jnp
from jax import lax
from jax.sharding import PartitionSpec as P

LAYERS = 1


def activate(values):
    return jax.nn.gelu(values, approximate=True)


def second_product(received, left):
    return jnp.einsum("ijt,jim->jmt", received, left, preferred_element_type=jnp.float32)


def left_apply(left, received):
    return (received, second_product(received, left))


def first_product(current, right):
    return jnp.einsum("ikt,ikj->ijt", current, right, preferred_element_type=jnp.float32).astype(
        jnp.bfloat16
    )


def forward_layer(current, right, left):
    first_out = first_product(current, right)
    return left_apply(
        left, lax.all_to_all(first_out, "mp", split_axis=1, concat_axis=0, tiled=True)
    )


def dp_stages(mesh):
    names = list(mesh.axis_names)
    devs = mesh.devices
    devs = devs.transpose([names.index("dp")] + [k for k in range(devs.ndim) if names[k] != "dp"])
    column = [devs[(d,) + (0,) * (devs.ndim - 1)] for d in range(devs.shape[0])]
    count = len(column)

    def key(dev):
        coords = tuple(getattr(dev, "coords", (dev.id,)))
        return coords + (getattr(dev, "core_on_chip", 0),)

    keys = [key(dev) for dev in column]
    stages = []
    stride = 1
    while stride < count:
        base = keys[0]
        step = keys[stride]
        varying = [a for a in range(len(base)) if base[a] != step[a]]
        size = 1
        while size * stride < count:
            probe = keys[size * stride]
            if [a for a in range(len(base)) if base[a] != probe[a]] != varying:
                break
            size += 1
        if count % (size * stride) != 0 or size < 2:
            size = count // stride
        distance = 0 if varying == [len(base) - 1] else max(
            abs(step[a] - base[a]) for a in varying
        )
        stages.append((distance, size, stride))
        stride *= size
    return stages


def staged_reduce_scatter(term, stages, count):
    lead = term.shape[:-2]
    rows, cols = term.shape[-2:]
    piece = rows // count
    by_stride = sorted(stages, key=lambda s: -s[2])
    digit_sizes = [s[1] for s in by_stride]
    x = term.reshape(lead + tuple(digit_sizes) + (piece, cols))
    order = sorted(stages, key=lambda s: (s[0], s[2]))
    nlead = len(lead)
    perm = [nlead + by_stride.index(s) for s in order]
    x = x.transpose(perm + list(range(nlead)) + list(range(nlead + len(stages), x.ndim)))
    inner = 1
    for extent in lead[1:]:
        inner *= extent
    x = x.reshape(x.shape[: len(stages)] + lead[:1] + (inner * piece, cols))
    me = lax.axis_index("dp")
    for distance, size, stride in order:
        mine = (me // stride) % size

        def pick(shift, x=x, mine=mine, size=size):
            return lax.dynamic_index_in_dim(x, (mine + shift) % size, 0, keepdims=False)

        def pairs(shift, size=size, stride=stride):
            out = []
            for d in range(count):
                own = (d // stride) % size
                out.append((d, d + (((own + shift) % size) - own) * stride))
            return out

        if size == 4 and distance > 1:
            wide = x.dtype
            ahead = jnp.stack([pick(1), pick(2)], 0).astype(jnp.bfloat16)
            ahead = lax.ppermute(ahead, "dp", perm=pairs(1))
            behind = lax.ppermute(pick(-1).astype(jnp.bfloat16), "dp", perm=pairs(-1))
            relayed = lax.ppermute(ahead[1], "dp", perm=pairs(1))
            x = pick(0) + ahead[0].astype(wide) + behind.astype(wide) + relayed.astype(wide)
            continue
        if size == 4:
            groups = []
            for d in range(count):
                if (d // stride) % size == 0:
                    groups.append([d + k * stride for k in range(size)])
            sent = lax.all_to_all(
                x.astype(jnp.bfloat16), "dp", 0, 0, tiled=True, axis_index_groups=groups
            )
            x = sent.astype(x.dtype).sum(0)
            continue
        total = pick(0)
        for shift in range(1, size):
            sent = lax.ppermute(pick(shift).astype(jnp.bfloat16), "dp", perm=pairs(shift))
            total = total + sent.astype(total.dtype)
        x = total
    return x.reshape(lead + (piece, cols))


def shards(stages, inputs, cotangent, r_factor, l_factor):
    block_count = r_factor.shape[1]
    block_size = r_factor.shape[2]
    tokens_here = inputs.shape[1]
    dp_count = lax.axis_size("dp")
    scale = float(dp_count * tokens_here) ** (-0.5)
    current = inputs.reshape(block_count, block_size, tokens_here)
    layer_index = 0
    received, pre_act = forward_layer(current, r_factor[layer_index], l_factor[layer_index])
    saved = [(current, received, pre_act)]
    current = activate(pre_act).astype(jnp.bfloat16)
    outputs = current.reshape(block_count * block_size, tokens_here)
    grad_now = cotangent.reshape(block_count, block_size, tokens_here)
    parts_r = [None] * LAYERS
    parts_l = [None] * LAYERS
    for layer_index in reversed(range(LAYERS)):
        right = r_factor[layer_index]
        left = l_factor[layer_index]
        layer_in = saved[layer_index][0]
        received = saved[layer_index][1]
        pre_act = saved[layer_index][2]
        back_fn = jax.vjp(activate, pre_act)[1]
        grad_pre = back_fn(grad_now.astype(jnp.float32))[0].astype(jnp.bfloat16)
        term_l = (
            jnp.einsum("ijt,jmt->jim", received, grad_pre, preferred_element_type=jnp.float32)
            * scale
        )
        grad_first = jnp.einsum(
            "jmt,jim->ijt", grad_pre, left, preferred_element_type=jnp.float32
        ).astype(jnp.bfloat16)

        def apply_back(returned, right=right):
            spread = jnp.einsum("ijt,ikj->ikt", returned, right, preferred_element_type=jnp.float32)
            return (returned, spread.astype(jnp.bfloat16))

        returned, grad_now = apply_back(
            lax.all_to_all(grad_first, "mp", split_axis=0, concat_axis=1, tiled=True)
        )
        term_r = (
            jnp.einsum("ikt,ijt->ikj", layer_in, returned, preferred_element_type=jnp.float32)
            * scale
        )
        both = staged_reduce_scatter(jnp.stack([term_l, term_r], 0), stages, dp_count)
        parts_l[layer_index] = both[0]
        parts_r[layer_index] = both[1]
    stack_r = jnp.stack(parts_r, 0)
    stack_l = jnp.stack(parts_l, 0)
    grad_inputs = grad_now.reshape(block_count * block_size, tokens_here)
    return (outputs, grad_inputs, stack_r, stack_l)


def solution(mesh):
    stages = dp_stages(mesh)
    placed = (P("mp", "dp"), P("mp", "dp"), P(None, "mp", None, None), P(None, "mp", None, None))

    def body(*args):
        return shards(stages, *args)

    return jax.shard_map(
        body,
        mesh=mesh,
        in_specs=placed,
        out_specs=(
            P("mp", "dp"),
            P("mp", "dp"),
            P(None, "mp", "dp", None),
            P(None, "mp", "dp", None),
        ),
        check_vma=False,
    )
```

```python
import jax
import jax.numpy as jnp
from jax import lax
from jax.sharding import PartitionSpec as P

LAYERS = 1


def activate(values):
    return jax.nn.gelu(values, approximate=True)


def second_product(received, left):
    return jnp.einsum("ijt,jim->jmt", received, left, preferred_element_type=jnp.float32)


def left_apply(left, received):
    return (received, second_product(received, left))


def first_product(current, right):
    return jnp.einsum("ikt,ikj->ijt", current, right, preferred_element_type=jnp.float32).astype(
        jnp.bfloat16
    )


def forward_layer(current, right, left):
    first_out = first_product(current, right)
    return left_apply(
        left, lax.all_to_all(first_out, "mp", split_axis=1, concat_axis=0, tiled=True)
    )


def dp_stages(mesh):
    names = list(mesh.axis_names)
    devs = mesh.devices
    devs = devs.transpose([names.index("dp")] + [k for k in range(devs.ndim) if names[k] != "dp"])
    column = [devs[(d,) + (0,) * (devs.ndim - 1)] for d in range(devs.shape[0])]
    count = len(column)

    def key(dev):
        coords = tuple(getattr(dev, "coords", (dev.id,)))
        return coords + (getattr(dev, "core_on_chip", 0),)

    keys = [key(dev) for dev in column]
    stages = []
    stride = 1
    while stride < count:
        base = keys[0]
        step = keys[stride]
        varying = [a for a in range(len(base)) if base[a] != step[a]]
        size = 1
        while size * stride < count:
            probe = keys[size * stride]
            if [a for a in range(len(base)) if base[a] != probe[a]] != varying:
                break
            size += 1
        if count % (size * stride) != 0 or size < 2:
            size = count // stride
        distance = 0 if varying == [len(base) - 1] else max(
            abs(step[a] - base[a]) for a in varying
        )
        stages.append((distance, size, stride))
        stride *= size
    return stages


def staged_reduce_scatter(term, stages, count):
    lead = term.shape[:-2]
    rows, cols = term.shape[-2:]
    piece = rows // count
    by_stride = sorted(stages, key=lambda s: -s[2])
    digit_sizes = [s[1] for s in by_stride]
    x = term.reshape(lead + tuple(digit_sizes) + (piece, cols))
    order = sorted(stages, key=lambda s: (s[0], s[2]))
    nlead = len(lead)
    perm = [nlead + by_stride.index(s) for s in order]
    x = x.transpose(perm + list(range(nlead)) + list(range(nlead + len(stages), x.ndim)))
    inner = 1
    for extent in lead[1:]:
        inner *= extent
    x = x.reshape(x.shape[: len(stages)] + lead[:1] + (inner * piece, cols))
    me = lax.axis_index("dp")
    for distance, size, stride in order:
        mine = (me // stride) % size

        def pick(shift, x=x, mine=mine, size=size):
            return lax.dynamic_index_in_dim(x, (mine + shift) % size, 0, keepdims=False)

        def pairs(shift, size=size, stride=stride):
            out = []
            for d in range(count):
                own = (d // stride) % size
                out.append((d, d + (((own + shift) % size) - own) * stride))
            return out

        if size == 4 and distance > 1:
            wide = x.dtype
            ahead = lax.ppermute(pick(2).astype(jnp.bfloat16), "dp", perm=pairs(1))
            behind = lax.ppermute(pick(-1).astype(jnp.bfloat16), "dp", perm=pairs(-1))
            carried = (ahead.astype(wide) + pick(1)).astype(jnp.bfloat16)
            relayed = lax.ppermute(carried, "dp", perm=pairs(1))
            x = pick(0) + behind.astype(wide) + relayed.astype(wide)
            continue
        if size == 4:
            groups = []
            for d in range(count):
                if (d // stride) % size == 0:
                    groups.append([d + k * stride for k in range(size)])
            sent = lax.all_to_all(
                x.astype(jnp.bfloat16), "dp", 0, 0, tiled=True, axis_index_groups=groups
            )
            x = sent.astype(x.dtype).sum(0)
            continue
        total = pick(0)
        for shift in range(1, size):
            sent = lax.ppermute(pick(shift).astype(jnp.bfloat16), "dp", perm=pairs(shift))
            total = total + sent.astype(total.dtype)
        x = total
    return x.reshape(lead + (piece, cols))


def shards(stages, inputs, cotangent, r_factor, l_factor):
    block_count = r_factor.shape[1]
    block_size = r_factor.shape[2]
    tokens_here = inputs.shape[1]
    dp_count = lax.axis_size("dp")
    scale = float(dp_count * tokens_here) ** (-0.5)
    current = inputs.reshape(block_count, block_size, tokens_here)
    layer_index = 0
    received, pre_act = forward_layer(current, r_factor[layer_index], l_factor[layer_index])
    saved = [(current, received, pre_act)]
    current = activate(pre_act).astype(jnp.bfloat16)
    outputs = current.reshape(block_count * block_size, tokens_here)
    grad_now = cotangent.reshape(block_count, block_size, tokens_here)
    parts_r = [None] * LAYERS
    parts_l = [None] * LAYERS
    for layer_index in reversed(range(LAYERS)):
        right = r_factor[layer_index]
        left = l_factor[layer_index]
        layer_in = saved[layer_index][0]
        received = saved[layer_index][1]
        pre_act = saved[layer_index][2]
        back_fn = jax.vjp(activate, pre_act)[1]
        grad_pre = back_fn(grad_now.astype(jnp.float32))[0].astype(jnp.bfloat16)
        term_l = (
            jnp.einsum("ijt,jmt->jim", received, grad_pre, preferred_element_type=jnp.float32)
            * scale
        )
        grad_first = jnp.einsum(
            "jmt,jim->ijt", grad_pre, left, preferred_element_type=jnp.float32
        ).astype(jnp.bfloat16)

        def apply_back(returned, right=right):
            spread = jnp.einsum("ijt,ikj->ikt", returned, right, preferred_element_type=jnp.float32)
            return (returned, spread.astype(jnp.bfloat16))

        returned, grad_now = apply_back(
            lax.all_to_all(grad_first, "mp", split_axis=0, concat_axis=1, tiled=True)
        )
        term_r = (
            jnp.einsum("ikt,ijt->ikj", layer_in, returned, preferred_element_type=jnp.float32)
            * scale
        )
        both = staged_reduce_scatter(jnp.stack([term_l, term_r], 0), stages, dp_count)
        parts_l[layer_index] = both[0]
        parts_r[layer_index] = both[1]
    stack_r = jnp.stack(parts_r, 0)
    stack_l = jnp.stack(parts_l, 0)
    grad_inputs = grad_now.reshape(block_count * block_size, tokens_here)
    return (outputs, grad_inputs, stack_r, stack_l)


def solution(mesh):
    stages = dp_stages(mesh)
    placed = (P("mp", "dp"), P("mp", "dp"), P(None, "mp", None, None), P(None, "mp", None, None))

    def body(*args):
        return shards(stages, *args)

    return jax.shard_map(
        body,
        mesh=mesh,
        in_specs=placed,
        out_specs=(
            P("mp", "dp"),
            P("mp", "dp"),
            P(None, "mp", "dp", None),
            P(None, "mp", "dp", None),
        ),
        check_vma=False,
    )
```

```python
import jax
import jax.numpy as jnp
from jax import lax
from jax.sharding import PartitionSpec as P

LAYERS = 1


def activate(values):
    return jax.nn.gelu(values, approximate=True)


def second_product(received, left):
    return jnp.einsum("ijt,jim->jmt", received, left, preferred_element_type=jnp.float32)


def left_apply(left, received):
    return (received, second_product(received, left))


def first_product(current, right):
    return jnp.einsum("ikt,ikj->ijt", current, right, preferred_element_type=jnp.float32).astype(
        jnp.bfloat16
    )


def forward_layer(current, right, left):
    first_out = first_product(current, right)
    return left_apply(
        left, lax.all_to_all(first_out, "mp", split_axis=1, concat_axis=0, tiled=True)
    )


def dp_stages(mesh):
    names = list(mesh.axis_names)
    devs = mesh.devices
    devs = devs.transpose([names.index("dp")] + [k for k in range(devs.ndim) if names[k] != "dp"])
    column = [devs[(d,) + (0,) * (devs.ndim - 1)] for d in range(devs.shape[0])]
    count = len(column)

    def key(dev):
        coords = tuple(getattr(dev, "coords", (dev.id,)))
        return coords + (getattr(dev, "core_on_chip", 0),)

    keys = [key(dev) for dev in column]
    stages = []
    stride = 1
    while stride < count:
        base = keys[0]
        step = keys[stride]
        varying = [a for a in range(len(base)) if base[a] != step[a]]
        size = 1
        while size * stride < count:
            probe = keys[size * stride]
            if [a for a in range(len(base)) if base[a] != probe[a]] != varying:
                break
            size += 1
        if count % (size * stride) != 0 or size < 2:
            size = count // stride
        distance = 0 if varying == [len(base) - 1] else max(
            abs(step[a] - base[a]) for a in varying
        )
        stages.append((distance, size, stride))
        stride *= size
    return stages


def stage_order(stages):
    return sorted(stages, key=lambda s: (s[0], s[2]))


def to_pieces(term, stages, count):
    blocks, rows, cols = term.shape
    piece = rows // count
    by_stride = sorted(stages, key=lambda s: -s[2])
    x = term.reshape((blocks,) + tuple(s[1] for s in by_stride) + (piece, cols))
    perm = [1 + by_stride.index(s) for s in stage_order(stages)]
    x = x.transpose(perm + [0, len(stages) + 1, len(stages) + 2])
    return x.reshape(x.shape[: len(stages)] + (blocks * piece, cols))


def reduce_stages(x, stages, count):
    me = lax.axis_index("dp")
    for distance, size, stride in stages:
        mine = (me // stride) % size

        def pick(shift, x=x, mine=mine, size=size):
            return lax.dynamic_index_in_dim(x, (mine + shift) % size, 0, keepdims=False)

        def pairs(shift, size=size, stride=stride):
            out = []
            for d in range(count):
                own = (d // stride) % size
                out.append((d, d + (((own + shift) % size) - own) * stride))
            return out

        if size == 4 and distance > 1:
            wide = x.dtype
            ahead = jnp.stack([pick(1), pick(2)], 0).astype(jnp.bfloat16)
            ahead = lax.ppermute(ahead, "dp", perm=pairs(1))
            behind = lax.ppermute(pick(-1).astype(jnp.bfloat16), "dp", perm=pairs(-1))
            relayed = lax.ppermute(ahead[1], "dp", perm=pairs(1))
            x = pick(0) + ahead[0].astype(wide) + behind.astype(wide) + relayed.astype(wide)
            continue
        if size == 4:
            groups = []
            for d in range(count):
                if (d // stride) % size == 0:
                    groups.append([d + k * stride for k in range(size)])
            sent = lax.all_to_all(
                x.astype(jnp.bfloat16), "dp", 0, 0, tiled=True, axis_index_groups=groups
            )
            x = sent.astype(x.dtype).sum(0)
            continue
        total = pick(0)
        for shift in range(1, size):
            sent = lax.ppermute(pick(shift).astype(jnp.bfloat16), "dp", perm=pairs(shift))
            total = total + sent.astype(total.dtype)
        x = total
    return x


def shards(stages, inputs, cotangent, r_factor, l_factor):
    block_count = r_factor.shape[1]
    block_size = r_factor.shape[2]
    tokens_here = inputs.shape[1]
    dp_count = lax.axis_size("dp")
    scale = float(dp_count * tokens_here) ** (-0.5)
    current = inputs.reshape(block_count, block_size, tokens_here)
    layer_index = 0
    received, pre_act = forward_layer(current, r_factor[layer_index], l_factor[layer_index])
    saved = [(current, received, pre_act)]
    current = activate(pre_act).astype(jnp.bfloat16)
    outputs = current.reshape(block_count * block_size, tokens_here)
    grad_now = cotangent.reshape(block_count, block_size, tokens_here)
    parts_r = [None] * LAYERS
    parts_l = [None] * LAYERS
    for layer_index in reversed(range(LAYERS)):
        right = r_factor[layer_index]
        left = l_factor[layer_index]
        layer_in = saved[layer_index][0]
        received = saved[layer_index][1]
        pre_act = saved[layer_index][2]
        back_fn = jax.vjp(activate, pre_act)[1]
        grad_pre = back_fn(grad_now.astype(jnp.float32))[0].astype(jnp.bfloat16)
        term_l = (
            jnp.einsum("ijt,jmt->jim", received, grad_pre, preferred_element_type=jnp.float32)
            * scale
        )
        order = stage_order(stages)
        early_l = reduce_stages(to_pieces(term_l, stages, dp_count), order[:1], dp_count)
        grad_first = jnp.einsum(
            "jmt,jim->ijt", grad_pre, left, preferred_element_type=jnp.float32
        ).astype(jnp.bfloat16)

        def apply_back(returned, right=right):
            spread = jnp.einsum("ijt,ikj->ikt", returned, right, preferred_element_type=jnp.float32)
            return (returned, spread.astype(jnp.bfloat16))

        returned, grad_now = apply_back(
            lax.all_to_all(grad_first, "mp", split_axis=0, concat_axis=1, tiled=True)
        )
        term_r = (
            jnp.einsum("ikt,ijt->ikj", layer_in, returned, preferred_element_type=jnp.float32)
            * scale
        )
        early_r = reduce_stages(to_pieces(term_r, stages, dp_count), order[:1], dp_count)
        both = jnp.stack([early_l, early_r], len(stages) - 1)
        both = reduce_stages(both, order[1:], dp_count)
        piece = block_size // dp_count
        parts_l[layer_index] = both[0].reshape(block_count, piece, block_size)
        parts_r[layer_index] = both[1].reshape(block_count, piece, block_size)
    stack_r = jnp.stack(parts_r, 0)
    stack_l = jnp.stack(parts_l, 0)
    grad_inputs = grad_now.reshape(block_count * block_size, tokens_here)
    return (outputs, grad_inputs, stack_r, stack_l)


def solution(mesh):
    stages = dp_stages(mesh)
    placed = (P("mp", "dp"), P("mp", "dp"), P(None, "mp", None, None), P(None, "mp", None, None))

    def body(*args):
        return shards(stages, *args)

    return jax.shard_map(
        body,
        mesh=mesh,
        in_specs=placed,
        out_specs=(
            P("mp", "dp"),
            P("mp", "dp"),
            P(None, "mp", "dp", None),
            P(None, "mp", "dp", None),
        ),
        check_vma=False,
    )
```

```python
import jax
import jax.numpy as jnp
from jax import lax
from jax.experimental import pallas as pl
from jax.sharding import PartitionSpec as P

LAYERS = 1


def activate(values):
    return jax.nn.gelu(values, approximate=True)


def second_product(received, left):
    return jnp.einsum("ijt,jim->jmt", received, left, preferred_element_type=jnp.float32)


def left_apply(left, received):
    return (received, second_product(received, left))


def first_kernel(current_ref, right_ref, out_ref):
    for block in range(current_ref.shape[0]):
        out_ref[block] = lax.dot_general(
            right_ref[block],
            current_ref[block],
            (((0,), (0,)), ((), ())),
            preferred_element_type=jnp.float32,
        ).astype(out_ref.dtype)


def first_product(current, right):
    blocks, _, tokens = current.shape
    width = right.shape[2]
    return pl.pallas_call(
        first_kernel,
        out_shape=jax.ShapeDtypeStruct((blocks, width, tokens), jnp.bfloat16),
    )(current, right)


def forward_layer(current, right, left):
    first_out = first_product(current, right)
    return left_apply(
        left, lax.all_to_all(first_out, "mp", split_axis=1, concat_axis=0, tiled=True)
    )


def dp_stages(mesh):
    names = list(mesh.axis_names)
    devs = mesh.devices
    devs = devs.transpose([names.index("dp")] + [k for k in range(devs.ndim) if names[k] != "dp"])
    column = [devs[(d,) + (0,) * (devs.ndim - 1)] for d in range(devs.shape[0])]
    count = len(column)

    def key(dev):
        coords = tuple(getattr(dev, "coords", (dev.id,)))
        return coords + (getattr(dev, "core_on_chip", 0),)

    keys = [key(dev) for dev in column]
    stages = []
    stride = 1
    while stride < count:
        base = keys[0]
        step = keys[stride]
        varying = [a for a in range(len(base)) if base[a] != step[a]]
        size = 1
        while size * stride < count:
            probe = keys[size * stride]
            if [a for a in range(len(base)) if base[a] != probe[a]] != varying:
                break
            size += 1
        if count % (size * stride) != 0 or size < 2:
            size = count // stride
        distance = 0 if varying == [len(base) - 1] else max(
            abs(step[a] - base[a]) for a in varying
        )
        stages.append((distance, size, stride))
        stride *= size
    return stages


def stage_order(stages):
    return sorted(stages, key=lambda s: (s[0], s[2]))


def to_pieces(term, stages, count):
    blocks, rows, cols = term.shape
    piece = rows // count
    by_stride = sorted(stages, key=lambda s: -s[2])
    x = term.reshape((blocks,) + tuple(s[1] for s in by_stride) + (piece, cols))
    perm = [1 + by_stride.index(s) for s in stage_order(stages)]
    x = x.transpose(perm + [0, len(stages) + 1, len(stages) + 2])
    return x.reshape(x.shape[: len(stages)] + (blocks * piece, cols))


def reduce_stages(x, stages, count):
    me = lax.axis_index("dp")
    for distance, size, stride in stages:
        mine = (me // stride) % size

        def pick(shift, x=x, mine=mine, size=size):
            return lax.dynamic_index_in_dim(x, (mine + shift) % size, 0, keepdims=False)

        def pairs(shift, size=size, stride=stride):
            out = []
            for d in range(count):
                own = (d // stride) % size
                out.append((d, d + (((own + shift) % size) - own) * stride))
            return out

        if size == 4 and distance > 1:
            wide = x.dtype
            ahead = jnp.stack([pick(1), pick(2)], 0).astype(jnp.bfloat16)
            ahead = lax.ppermute(ahead, "dp", perm=pairs(1))
            behind = lax.ppermute(pick(-1).astype(jnp.bfloat16), "dp", perm=pairs(-1))
            relayed = lax.ppermute(ahead[1], "dp", perm=pairs(1))
            x = pick(0) + ahead[0].astype(wide) + behind.astype(wide) + relayed.astype(wide)
            continue
        if size == 4:
            groups = []
            for d in range(count):
                if (d // stride) % size == 0:
                    groups.append([d + k * stride for k in range(size)])
            sent = lax.all_to_all(
                x.astype(jnp.bfloat16), "dp", 0, 0, tiled=True, axis_index_groups=groups
            )
            x = sent.astype(x.dtype).sum(0)
            continue
        total = pick(0)
        for shift in range(1, size):
            sent = lax.ppermute(pick(shift).astype(jnp.bfloat16), "dp", perm=pairs(shift))
            total = total + sent.astype(total.dtype)
        x = total
    return x


def shards(stages, inputs, cotangent, r_factor, l_factor):
    block_count = r_factor.shape[1]
    block_size = r_factor.shape[2]
    tokens_here = inputs.shape[1]
    dp_count = lax.axis_size("dp")
    scale = float(dp_count * tokens_here) ** (-0.5)
    current = inputs.reshape(block_count, block_size, tokens_here)
    layer_index = 0
    received, pre_act = forward_layer(current, r_factor[layer_index], l_factor[layer_index])
    saved = [(current, received, pre_act)]
    current = activate(pre_act).astype(jnp.bfloat16)
    outputs = current.reshape(block_count * block_size, tokens_here)
    grad_now = cotangent.reshape(block_count, block_size, tokens_here)
    parts_r = [None] * LAYERS
    parts_l = [None] * LAYERS
    for layer_index in reversed(range(LAYERS)):
        right = r_factor[layer_index]
        left = l_factor[layer_index]
        layer_in = saved[layer_index][0]
        received = saved[layer_index][1]
        pre_act = saved[layer_index][2]
        back_fn = jax.vjp(activate, pre_act)[1]
        grad_pre = back_fn(grad_now.astype(jnp.float32))[0].astype(jnp.bfloat16)
        term_l = (
            jnp.einsum("ijt,jmt->jim", received, grad_pre, preferred_element_type=jnp.float32)
            * scale
        )
        order = stage_order(stages)
        early_l = reduce_stages(to_pieces(term_l, stages, dp_count), order[:1], dp_count)
        grad_first = jnp.einsum(
            "jmt,jim->ijt", grad_pre, left, preferred_element_type=jnp.float32
        ).astype(jnp.bfloat16)

        def apply_back(returned, right=right):
            spread = jnp.einsum("ijt,ikj->ikt", returned, right, preferred_element_type=jnp.float32)
            return (returned, spread.astype(jnp.bfloat16))

        returned, grad_now = apply_back(
            lax.all_to_all(grad_first, "mp", split_axis=0, concat_axis=1, tiled=True)
        )
        term_r = (
            jnp.einsum("ikt,ijt->ikj", layer_in, returned, preferred_element_type=jnp.float32)
            * scale
        )
        early_r = reduce_stages(to_pieces(term_r, stages, dp_count), order[:1], dp_count)
        both = jnp.stack([early_l, early_r], len(stages) - 1)
        both = reduce_stages(both, order[1:], dp_count)
        piece = block_size // dp_count
        parts_l[layer_index] = both[0].reshape(block_count, piece, block_size)
        parts_r[layer_index] = both[1].reshape(block_count, piece, block_size)
    stack_r = jnp.stack(parts_r, 0)
    stack_l = jnp.stack(parts_l, 0)
    grad_inputs = grad_now.reshape(block_count * block_size, tokens_here)
    return (outputs, grad_inputs, stack_r, stack_l)


def solution(mesh):
    stages = dp_stages(mesh)
    placed = (P("mp", "dp"), P("mp", "dp"), P(None, "mp", None, None), P(None, "mp", None, None))

    def body(*args):
        return shards(stages, *args)

    return jax.shard_map(
        body,
        mesh=mesh,
        in_specs=placed,
        out_specs=(
            P("mp", "dp"),
            P("mp", "dp"),
            P(None, "mp", "dp", None),
            P(None, "mp", "dp", None),
        ),
        check_vma=False,
    )
```

```python
import jax
import jax.numpy as jnp
from jax import lax
from jax.sharding import PartitionSpec as P

LAYERS = 1


def activate(values):
    return jax.nn.gelu(values, approximate=True)


def second_product(received, left):
    return jnp.einsum("ijt,jim->jmt", received, left, preferred_element_type=jnp.float32)


def left_apply(left, received):
    return (received, second_product(received, left))


def first_product(current, right):
    return jnp.einsum("ikt,ikj->ijt", current, right, preferred_element_type=jnp.float32).astype(
        jnp.bfloat16
    )


def forward_layer(current, right, left):
    first_out = first_product(current, right)
    return left_apply(
        left, lax.all_to_all(first_out, "mp", split_axis=1, concat_axis=0, tiled=True)
    )


def dp_stages(mesh):
    names = list(mesh.axis_names)
    devs = mesh.devices
    devs = devs.transpose([names.index("dp")] + [k for k in range(devs.ndim) if names[k] != "dp"])
    column = [devs[(d,) + (0,) * (devs.ndim - 1)] for d in range(devs.shape[0])]
    count = len(column)

    def key(dev):
        coords = tuple(getattr(dev, "coords", (dev.id,)))
        return coords + (getattr(dev, "core_on_chip", 0),)

    keys = [key(dev) for dev in column]
    stages = []
    stride = 1
    while stride < count:
        base = keys[0]
        step = keys[stride]
        varying = [a for a in range(len(base)) if base[a] != step[a]]
        size = 1
        while size * stride < count:
            probe = keys[size * stride]
            if [a for a in range(len(base)) if base[a] != probe[a]] != varying:
                break
            size += 1
        if count % (size * stride) != 0 or size < 2:
            size = count // stride
        distance = 0 if varying == [len(base) - 1] else max(
            abs(step[a] - base[a]) for a in varying
        )
        stages.append((distance, size, stride))
        stride *= size
    return stages


def stage_order(stages):
    return sorted(stages, key=lambda s: (s[0], s[2]))


def to_pieces(term, stages, count):
    blocks, rows, cols = term.shape
    piece = rows // count
    by_stride = sorted(stages, key=lambda s: -s[2])
    x = term.reshape((blocks,) + tuple(s[1] for s in by_stride) + (piece, cols))
    perm = [1 + by_stride.index(s) for s in stage_order(stages)]
    x = x.transpose(perm + [0, len(stages) + 1, len(stages) + 2])
    return x.reshape(x.shape[: len(stages)] + (blocks * piece, cols))


def reduce_stages(x, stages, count):
    me = lax.axis_index("dp")
    for distance, size, stride in stages:
        mine = (me // stride) % size

        def pick(shift, x=x, mine=mine, size=size):
            return lax.dynamic_index_in_dim(x, (mine + shift) % size, 0, keepdims=False)

        def pairs(shift, size=size, stride=stride):
            out = []
            for d in range(count):
                own = (d // stride) % size
                out.append((d, d + (((own + shift) % size) - own) * stride))
            return out

        if size == 4 and distance > 1:
            wide = x.dtype
            ahead = jnp.stack([pick(1), pick(2)], 0).astype(jnp.bfloat16)
            ahead = lax.ppermute(ahead, "dp", perm=pairs(1))
            behind = lax.ppermute(pick(-1).astype(jnp.bfloat16), "dp", perm=pairs(-1))
            relayed = lax.ppermute(ahead[1], "dp", perm=pairs(1))
            x = pick(0) + ahead[0].astype(wide) + behind.astype(wide) + relayed.astype(wide)
            continue
        if size == 4:
            groups = []
            for d in range(count):
                if (d // stride) % size == 0:
                    groups.append([d + k * stride for k in range(size)])
            sent = lax.all_to_all(
                x.astype(jnp.bfloat16), "dp", 0, 0, tiled=True, axis_index_groups=groups
            )
            x = sent.astype(x.dtype).sum(0)
            continue
        total = pick(0)
        for shift in range(1, size):
            sent = lax.ppermute(pick(shift).astype(jnp.bfloat16), "dp", perm=pairs(shift))
            total = total + sent.astype(total.dtype)
        x = total
    return x


def shards(stages, inputs, cotangent, r_factor, l_factor):
    block_count = r_factor.shape[1]
    block_size = r_factor.shape[2]
    tokens_here = inputs.shape[1]
    dp_count = lax.axis_size("dp")
    scale = float(dp_count * tokens_here) ** (-0.5)
    current = inputs.reshape(block_count, block_size, tokens_here)
    layer_index = 0
    received, pre_act = forward_layer(current, r_factor[layer_index], l_factor[layer_index])
    saved = [(current, received, pre_act)]
    current = activate(pre_act).astype(jnp.bfloat16)
    outputs = current.reshape(block_count * block_size, tokens_here)
    grad_now = cotangent.reshape(block_count, block_size, tokens_here)
    parts_r = [None] * LAYERS
    parts_l = [None] * LAYERS
    for layer_index in reversed(range(LAYERS)):
        right = r_factor[layer_index]
        left = l_factor[layer_index]
        layer_in = saved[layer_index][0]
        received = saved[layer_index][1]
        pre_act = saved[layer_index][2]
        back_fn = jax.vjp(activate, pre_act)[1]
        grad_pre = back_fn(grad_now.astype(jnp.float32))[0].astype(jnp.bfloat16)
        term_l = (
            jnp.einsum("ijt,jmt->jim", received, grad_pre, preferred_element_type=jnp.float32)
            * scale
        )
        order = stage_order(stages)
        early_l = reduce_stages(to_pieces(term_l, stages, dp_count), order[:1], dp_count)
        grad_first = jnp.einsum(
            "jmt,jim->ijt", grad_pre, left, preferred_element_type=jnp.float32
        ).astype(jnp.bfloat16)

        def apply_back(returned, right=right):
            spread = jnp.einsum("ijt,ikj->ikt", returned, right, preferred_element_type=jnp.float32)
            return (returned, spread.astype(jnp.bfloat16))

        returned, grad_now = apply_back(
            lax.all_to_all(grad_first, "mp", split_axis=0, concat_axis=1, tiled=True)
        )
        term_r = (
            jnp.einsum("ikt,ijt->ikj", layer_in, returned, preferred_element_type=jnp.float32)
            * scale
        )
        early_r = reduce_stages(to_pieces(term_r, stages, dp_count), order[:1], dp_count)
        both = jnp.concatenate([early_l, early_r], -2)
        both = reduce_stages(both, order[1:], dp_count)
        piece = block_size // dp_count
        half = block_count * piece
        parts_l[layer_index] = both[:half].reshape(block_count, piece, block_size)
        parts_r[layer_index] = both[half:].reshape(block_count, piece, block_size)
    stack_r = jnp.stack(parts_r, 0)
    stack_l = jnp.stack(parts_l, 0)
    grad_inputs = grad_now.reshape(block_count * block_size, tokens_here)
    return (outputs, grad_inputs, stack_r, stack_l)


def solution(mesh):
    stages = dp_stages(mesh)
    placed = (P("mp", "dp"), P("mp", "dp"), P(None, "mp", None, None), P(None, "mp", None, None))

    def body(*args):
        return shards(stages, *args)

    return jax.shard_map(
        body,
        mesh=mesh,
        in_specs=placed,
        out_specs=(
            P("mp", "dp"),
            P("mp", "dp"),
            P(None, "mp", "dp", None),
            P(None, "mp", "dp", None),
        ),
        check_vma=False,
    )
```

```python
import jax
import jax.numpy as jnp
from jax import lax
from jax.sharding import PartitionSpec as P

LAYERS = 1


def activate(values):
    return jax.nn.gelu(values, approximate=True)


def second_product(received, left):
    return jnp.einsum("ijt,jim->jmt", received, left, preferred_element_type=jnp.float32)


def left_apply(left, received):
    return (received, second_product(received, left))


def first_product(current, right):
    return jnp.einsum("ikt,ikj->ijt", current, right, preferred_element_type=jnp.float32).astype(
        jnp.bfloat16
    )


def forward_layer(current, right, left):
    first_out = first_product(current, right)
    return left_apply(
        left, lax.all_to_all(first_out, "mp", split_axis=1, concat_axis=0, tiled=True)
    )


def dp_stages(mesh):
    names = list(mesh.axis_names)
    devs = mesh.devices
    devs = devs.transpose([names.index("dp")] + [k for k in range(devs.ndim) if names[k] != "dp"])
    column = [devs[(d,) + (0,) * (devs.ndim - 1)] for d in range(devs.shape[0])]
    count = len(column)

    def key(dev):
        coords = tuple(getattr(dev, "coords", (dev.id,)))
        return coords + (getattr(dev, "core_on_chip", 0),)

    keys = [key(dev) for dev in column]
    stages = []
    stride = 1
    while stride < count:
        base = keys[0]
        step = keys[stride]
        varying = [a for a in range(len(base)) if base[a] != step[a]]
        size = 1
        while size * stride < count:
            probe = keys[size * stride]
            if [a for a in range(len(base)) if base[a] != probe[a]] != varying:
                break
            size += 1
        if count % (size * stride) != 0 or size < 2:
            size = count // stride
        distance = 0 if varying == [len(base) - 1] else max(
            abs(step[a] - base[a]) for a in varying
        )
        stages.append((distance, size, stride))
        stride *= size
    return stages


def stage_order(stages):
    return sorted(stages, key=lambda s: (s[0], s[2]))


def to_pieces(term, stages, count):
    blocks, rows, cols = term.shape
    piece = rows // count
    by_stride = sorted(stages, key=lambda s: -s[2])
    x = term.reshape((blocks,) + tuple(s[1] for s in by_stride) + (piece, cols))
    perm = [1 + by_stride.index(s) for s in stage_order(stages)]
    x = x.transpose(perm + [0, len(stages) + 1, len(stages) + 2])
    return x.reshape(x.shape[: len(stages)] + (blocks * piece, cols))


def reduce_stages(x, stages, count):
    me = lax.axis_index("dp")
    for distance, size, stride in stages:
        mine = (me // stride) % size

        def pick(shift, x=x, mine=mine, size=size):
            return lax.dynamic_index_in_dim(x, (mine + shift) % size, 0, keepdims=False)

        def pairs(shift, size=size, stride=stride):
            out = []
            for d in range(count):
                own = (d // stride) % size
                out.append((d, d + (((own + shift) % size) - own) * stride))
            return out

        if size == 4 and distance > 1:
            wide = x.dtype
            ahead = jnp.stack([pick(1), pick(2)], 0).astype(jnp.bfloat16)
            ahead = lax.ppermute(ahead, "dp", perm=pairs(1))
            behind = lax.ppermute(pick(-1).astype(jnp.bfloat16), "dp", perm=pairs(-1))
            relayed = lax.ppermute(ahead[1], "dp", perm=pairs(1))
            x = pick(0) + ahead[0].astype(wide) + behind.astype(wide) + relayed.astype(wide)
            continue
        if size == 4:
            groups = []
            for d in range(count):
                if (d // stride) % size == 0:
                    groups.append([d + k * stride for k in range(size)])
            sent = lax.all_to_all(
                x.astype(jnp.bfloat16), "dp", 0, 0, tiled=True, axis_index_groups=groups
            )
            x = sent.astype(x.dtype).sum(0)
            continue
        total = pick(0)
        for shift in range(1, size):
            sent = lax.ppermute(pick(shift).astype(jnp.bfloat16), "dp", perm=pairs(shift))
            total = total + sent.astype(total.dtype)
        x = total
    return x


def shards(stages, inputs, cotangent, r_factor, l_factor):
    block_count = r_factor.shape[1]
    block_size = r_factor.shape[2]
    tokens_here = inputs.shape[1]
    dp_count = lax.axis_size("dp")
    scale = float(dp_count * tokens_here) ** (-0.5)
    current = inputs.reshape(block_count, block_size, tokens_here)
    layer_index = 0
    received, pre_act = forward_layer(current, r_factor[layer_index], l_factor[layer_index])
    saved = [(current, received, pre_act)]
    current = activate(pre_act).astype(jnp.bfloat16)
    outputs = current.reshape(block_count * block_size, tokens_here)
    grad_now = cotangent.reshape(block_count, block_size, tokens_here)
    parts_r = [None] * LAYERS
    parts_l = [None] * LAYERS
    for layer_index in reversed(range(LAYERS)):
        right = r_factor[layer_index]
        left = l_factor[layer_index]
        layer_in = saved[layer_index][0]
        received = saved[layer_index][1]
        pre_act = saved[layer_index][2]
        back_fn = jax.vjp(activate, pre_act)[1]
        grad_pre = back_fn(grad_now.astype(jnp.float32))[0].astype(jnp.bfloat16)
        term_l = (
            jnp.einsum("ijt,jmt->jim", received, grad_pre, preferred_element_type=jnp.float32)
            * scale
        )
        order = stage_order(stages)
        early_l = reduce_stages(to_pieces(term_l, stages, dp_count), order[:1], dp_count)
        owners = lax.axis_size("mp")
        left_split = left.reshape(block_count, owners, block_size // owners, block_size)
        grad_first = jnp.einsum(
            "jpam,jmt->pjat", left_split, grad_pre, preferred_element_type=jnp.float32
        ).astype(jnp.bfloat16)
        grad_first = grad_first.transpose(0, 2, 1, 3).reshape(block_size, block_count, tokens_here)

        def apply_back(returned, right=right):
            spread = jnp.einsum("ijt,ikj->ikt", returned, right, preferred_element_type=jnp.float32)
            return (returned, spread.astype(jnp.bfloat16))

        returned, grad_now = apply_back(
            lax.all_to_all(grad_first, "mp", split_axis=0, concat_axis=1, tiled=True)
        )
        term_r = (
            jnp.einsum("ikt,ijt->ikj", layer_in, returned, preferred_element_type=jnp.float32)
            * scale
        )
        early_r = reduce_stages(to_pieces(term_r, stages, dp_count), order[:1], dp_count)
        both = jnp.concatenate([early_l, early_r], -2)
        both = reduce_stages(both, order[1:], dp_count)
        piece = block_size // dp_count
        half = block_count * piece
        parts_l[layer_index] = both[:half].reshape(block_count, piece, block_size)
        parts_r[layer_index] = both[half:].reshape(block_count, piece, block_size)
    stack_r = jnp.stack(parts_r, 0)
    stack_l = jnp.stack(parts_l, 0)
    grad_inputs = grad_now.reshape(block_count * block_size, tokens_here)
    return (outputs, grad_inputs, stack_r, stack_l)


def solution(mesh):
    stages = dp_stages(mesh)
    placed = (P("mp", "dp"), P("mp", "dp"), P(None, "mp", None, None), P(None, "mp", None, None))

    def body(*args):
        return shards(stages, *args)

    return jax.shard_map(
        body,
        mesh=mesh,
        in_specs=placed,
        out_specs=(
            P("mp", "dp"),
            P("mp", "dp"),
            P(None, "mp", "dp", None),
            P(None, "mp", "dp", None),
        ),
        check_vma=False,
    )
```
